128 devices in a mesh: dp: 2 (over core), cent: 64 (over z, y, x).
Axes of the slice: x: 4, y: 4, z: 4, core: 2. Of those that a mesh axis runs over, the one named last changes fastest.
Arguments:
- points: bfloat16 [16384, 768], P(('dp', 'cent')), may hold values from -16 to 16
- centroids: float32 [32768, 768], P(('dp', 'cent')), may hold values from -1.5 to 1.5
Outputs:
- new_centroids: float32 [32768, 768], P(('dp', 'cent'))
- log_total: float32 [16384], P(('dp', 'cent'))
The draws below stay inside these ranges and needn't reach their ends.
All inputs are finite; a program needn't handle non-finite values.
Results may differ from the reference program's by a relative error of at most 0.0088.
Values may be sent and summed in bfloat16 or wider, within the bound.
No kernel may reach another device: no remote copies, remote signals or barrier semaphores. Data moves between devices by JAX's collectives and lax.ppermute only.
A program may use at most 128 MiB of HBM per device.

```python
import math
import jax
import jax.numpy as jnp
from jax import lax

D = 768
K = 32768
NPTS = 16384


pair_count = 6


def centroid_table(key):
    first_key = jax.random.fold_in(key, 11)
    table = jax.random.normal(first_key, (K, D), jnp.float32) * 0.25
    return jnp.clip(table, -1.5, 1.5)


def draw_centroids(key, part):
    return centroid_table(key)


def aligned_rows(key, values):
    table = centroid_table(key)
    chosen = jax.random.randint(jax.random.fold_in(key, 12), (pair_count,), 0, K - 1)
    targets = jax.random.randint(jax.random.fold_in(key, 24), (pair_count,), 0, NPTS)
    rows = table[chosen]
    row_norm = jnp.sum(rows * rows, axis=1)
    wanted = jnp.array([120.0, 160.0, 220.0, 120.0, 160.0, 220.0], jnp.float32)
    strength = (wanted * math.sqrt(D) / (7.0 * row_norm) + 1.0) * 0.5
    return values.at[targets].set(rows * strength[:, None])


def draw_points(key, part):
    row_scale = jnp.exp(jax.random.uniform(jax.random.fold_in(key, 21), (NPTS, 1), jnp.float32, -1.0498221, 1.252763))
    values = jax.random.normal(jax.random.fold_in(key, 22), (NPTS, D), jnp.float32) * row_scale
    values = aligned_rows(key, values)
    return jnp.clip(values, -16.0, 16.0).astype(jnp.bfloat16)


def setup_inputs(seed: int = 0) -> dict:
    splits = jax.random.split(jax.random.key(seed), 3)
    points = draw_points(jax.random.fold_in(splits[2], 71), 0)
    centroids = draw_centroids(jax.random.fold_in(splits[2], 71), 0)
    return dict(points=points, centroids=centroids)


def fold_stats(running, scores):
    old_max, old_sum = running
    new_max = jnp.maximum(old_max, lax.optimization_barrier(jnp.max(scores, axis=1)))
    new_sum = old_sum * jnp.exp(old_max - new_max) + lax.optimization_barrier(jnp.sum(jnp.exp(scores - new_max[:, None]), axis=1))
    return (new_max, new_sum)

def reference(points, centroids):
    copies = centroids.astype(jnp.bfloat16)
    copies = lax.optimization_barrier(copies).astype(jnp.float32)
    sq_norm = lax.optimization_barrier(jnp.sum(copies * copies, axis=1))
    features = points.astype(jnp.float32)
    score_scale = 7.0 / math.sqrt(D)
    block_count = K // 512
    stacked = copies.reshape(block_count, 512, D)
    norm_rows = sq_norm.reshape(block_count, 512)

    def scores_of(table, norms):
        products = jnp.dot(features, table.T, precision=lax.Precision.HIGHEST)
        return (2.0 * products - norms[None, :]) * score_scale

    def scan_step(running, item):
        table, norms = item
        return (fold_stats(running, scores_of(table, norms)), None)
    start = (jnp.full((NPTS,), -1e+30, jnp.float32), jnp.zeros((NPTS,), jnp.float32))
    (run_max, run_sum), unused = lax.scan(scan_step, start, (stacked, norm_rows))
    log_total = run_max + jnp.log(run_sum)

    def block_sums(item):
        table, norms = item
        weights = jnp.exp(scores_of(table, norms) - log_total[:, None]).astype(jnp.bfloat16)
        weights = lax.optimization_barrier(weights).astype(jnp.float32)
        return (jnp.dot(weights.T, features, precision=lax.Precision.HIGHEST), lax.optimization_barrier(jnp.sum(weights, axis=0)))
    sums, counts = lax.map(block_sums, (stacked, norm_rows))
    sums = sums.reshape(K, D)
    counts = counts.reshape(K)
    new_centroids = (sums + centroids) / (counts[:, None] + 1.0)
    return (new_centroids, log_total)
```

```python
import math

import jax
import jax.numpy as jnp
from jax import lax
from jax.sharding import PartitionSpec as P

BLOCKS = 2


def score_block(members, cent_block, score_scale):
    sq_norm = jnp.sum(jnp.square(cent_block.astype(jnp.float32)), axis=1)
    products = lax.dot_general(
        members, cent_block, (((1,), (1,)), ((), ())), preferred_element_type=jnp.float32
    )
    return (2.0 * products - sq_norm[None, :]) * score_scale


def fold_stats(running, scores):
    old_max, old_sum = running
    new_max = jnp.maximum(old_max, jnp.max(scores, axis=1))
    new_sum = old_sum * jnp.exp(old_max - new_max) + jnp.sum(
        jnp.exp(scores - new_max[:, None]), axis=1
    )
    return (new_max, new_sum)


def group_log_total(local_max, local_sum, own_points):
    cent_count = lax.axis_size("cent")
    packed = jnp.stack(
        [local_max.reshape(cent_count, own_points), local_sum.reshape(cent_count, own_points)], axis=1
    )
    parts = lax.all_to_all(packed, "cent", 0, 0, tiled=True)
    part_max, part_sum = parts[:, 0], parts[:, 1]
    top = jnp.max(part_max, axis=0)
    total = jnp.sum(part_sum * jnp.exp(part_max - top[None, :]), axis=0)
    own_total = top + jnp.log(total)
    spread = jnp.broadcast_to(own_total[None], (cent_count, own_points))
    log_total = lax.all_to_all(spread, "cent", 0, 0, tiled=True).reshape(cent_count * own_points)
    return own_total, log_total


def on_device(points, centroids):
    feature_width = centroids.shape[1]
    own_rows = centroids.shape[0]
    dp_count = lax.axis_size("dp")
    score_scale = 7.0 / math.sqrt(feature_width)
    copies = centroids.astype(jnp.bfloat16)
    members = lax.all_gather(points, "cent", axis=0, tiled=True)
    member_rows = members.shape[0]
    start = (jnp.full((member_rows,), -1e30, jnp.float32), jnp.zeros((member_rows,), jnp.float32))
    part_rows = own_rows // BLOCKS
    gathered = lax.all_gather(copies, "dp", axis=0, tiled=True)
    running = start
    block_span = gathered.shape[0] // BLOCKS
    for index_j in range(BLOCKS):
        running = fold_stats(
            running,
            score_block(
                members, gathered[index_j * block_span : (index_j + 1) * block_span], score_scale
            ),
        )
    local_max, local_sum = running
    own_total, log_total = group_log_total(local_max, local_sum, points.shape[0])
    arranged = gathered.reshape(dp_count, BLOCKS, part_rows, feature_width)
    sum_parts = []
    count_parts = []
    for index_j in range(BLOCKS):
        cent_block = arranged[:, index_j].reshape(dp_count * part_rows, feature_width)
        scores = score_block(members, cent_block, score_scale)
        weights = jnp.exp(scores - log_total[:, None]).astype(jnp.bfloat16)
        partial_sums = lax.dot_general(
            weights, members, (((0,), (0,)), ((), ())), preferred_element_type=jnp.float32
        )
        counts = jnp.sum(weights, axis=0, dtype=jnp.float32)
        owned_sums, owned_counts = (
            lax.psum_scatter(partial_sums, "dp", scatter_dimension=0, tiled=True),
            lax.psum_scatter(counts, "dp", scatter_dimension=0, tiled=True),
        )
        sum_parts.append(owned_sums)
        count_parts.append(owned_counts)
    own_sums = jnp.concatenate(sum_parts, axis=0)
    own_counts = jnp.concatenate(count_parts, axis=0)
    new_centroids = (own_sums + centroids) / (own_counts[:, None] + 1.0)
    return (new_centroids, own_total)


def solution(mesh):
    placed = (P(("dp", "cent"), None), P(("dp", "cent"), None))
    return jax.shard_map(
        on_device,
        mesh=mesh,
        in_specs=placed,
        out_specs=(P(("dp", "cent"), None), P(("dp", "cent"))),
        check_vma=False,
    )
```

```python
import math

import jax
import jax.numpy as jnp
from jax import lax
from jax.sharding import PartitionSpec as P

HALVES = 2


def score_block(members, cent_block, score_scale):
    sq_norm = jnp.sum(jnp.square(cent_block.astype(jnp.float32)), axis=1)
    products = lax.dot_general(
        members, cent_block, (((1,), (1,)), ((), ())), preferred_element_type=jnp.float32
    )
    return (2.0 * products - sq_norm[None, :]) * score_scale


def group_log_total(local_max, local_sum, own_points):
    cent_count = lax.axis_size("cent")
    packed = jnp.stack(
        [local_max.reshape(cent_count, own_points), local_sum.reshape(cent_count, own_points)], axis=1
    )
    parts = lax.all_to_all(packed, "cent", 0, 0, tiled=True)
    part_max, part_sum = parts[:, 0], parts[:, 1]
    top = jnp.max(part_max, axis=0)
    total = jnp.sum(part_sum * jnp.exp(part_max - top[None, :]), axis=0)
    own_total = top + jnp.log(total)
    spread = jnp.broadcast_to(own_total[None], (cent_count, own_points))
    log_total = lax.all_to_all(spread, "cent", 0, 0, tiled=True).reshape(cent_count * own_points)
    return own_total, log_total


def on_device(points, centroids):
    feature_width = centroids.shape[1]
    own_points = points.shape[0]
    cent_count = lax.axis_size("cent")
    score_scale = 7.0 / math.sqrt(feature_width)
    copies = centroids.astype(jnp.bfloat16)
    members = lax.all_gather(points, "cent", axis=0, tiled=True)
    gathered = lax.all_gather(copies, "dp", axis=0, tiled=True)
    half_points = own_points // HALVES
    split = members.reshape(cent_count, HALVES, half_points, feature_width)
    own_parts = []
    sums = None
    counts = None
    for index_h in range(HALVES):
        half = split[:, index_h].reshape(cent_count * half_points, feature_width)
        scores = score_block(half, gathered, score_scale)
        local_max = jnp.max(scores, axis=1)
        local_sum = jnp.sum(jnp.exp(scores - local_max[:, None]), axis=1)
        own_total, log_total = group_log_total(local_max, local_sum, half_points)
        own_parts.append(own_total)
        weights = jnp.exp(scores - log_total[:, None]).astype(jnp.bfloat16)
        part_sums = lax.dot_general(
            weights, half, (((0,), (0,)), ((), ())), preferred_element_type=jnp.float32
        )
        part_counts = jnp.sum(weights, axis=0, dtype=jnp.float32)
        sums = part_sums if sums is None else sums + part_sums
        counts = part_counts if counts is None else counts + part_counts
    own_sums = lax.psum_scatter(sums, "dp", scatter_dimension=0, tiled=True)
    own_counts = lax.psum_scatter(counts, "dp", scatter_dimension=0, tiled=True)
    new_centroids = (own_sums + centroids) / (own_counts[:, None] + 1.0)
    return (new_centroids, jnp.concatenate(own_parts))


def solution(mesh):
    placed = (P(("dp", "cent"), None), P(("dp", "cent"), None))
    return jax.shard_map(
        on_device,
        mesh=mesh,
        in_specs=placed,
        out_specs=(P(("dp", "cent"), None), P(("dp", "cent"))),
        check_vma=False,
    )
```

```python
import math

import jax
import jax.numpy as jnp
from jax import lax
from jax.sharding import PartitionSpec as P


def score_block(members, cent_block, score_scale):
    sq_norm = jnp.sum(jnp.square(cent_block.astype(jnp.float32)), axis=1)
    products = lax.dot_general(
        members, cent_block, (((1,), (1,)), ((), ())), preferred_element_type=jnp.float32
    )
    return (2.0 * products - sq_norm[None, :]) * score_scale


def group_log_total(local_max, local_sum, own_points):
    cent_count = lax.axis_size("cent")
    packed = jnp.stack(
        [local_max.reshape(cent_count, own_points), local_sum.reshape(cent_count, own_points)], axis=1
    )
    parts = lax.all_to_all(packed, "cent", 0, 0, tiled=True)
    part_max, part_sum = parts[:, 0], parts[:, 1]
    top = jnp.max(part_max, axis=0)
    total = jnp.sum(part_sum * jnp.exp(part_max - top[None, :]), axis=0)
    own_total = top + jnp.log(total)
    spread = jnp.broadcast_to(own_total[None], (cent_count, own_points))
    log_total = lax.all_to_all(spread, "cent", 0, 0, tiled=True).reshape(cent_count * own_points)
    return own_total, log_total


def block_sums(scores, log_total, members):
    weights = jnp.exp(scores - log_total[:, None]).astype(jnp.bfloat16)
    sums = lax.dot_general(
        weights, members, (((0,), (0,)), ((), ())), preferred_element_type=jnp.float32
    )
    counts = jnp.sum(weights, axis=0, dtype=jnp.float32)
    return sums, counts


def on_device(points, centroids):
    feature_width = centroids.shape[1]
    score_scale = 7.0 / math.sqrt(feature_width)
    swap = [(0, 1), (1, 0)]
    copies = centroids.astype(jnp.bfloat16)
    members = lax.all_gather(points, "cent", axis=0, tiled=True)
    other_copies = lax.ppermute(copies, "dp", swap)
    other_scores = score_block(members, other_copies, score_scale)
    own_scores = score_block(members, copies, score_scale)
    local_max = jnp.maximum(jnp.max(other_scores, axis=1), jnp.max(own_scores, axis=1))
    local_sum = jnp.sum(jnp.exp(other_scores - local_max[:, None]), axis=1) + jnp.sum(
        jnp.exp(own_scores - local_max[:, None]), axis=1
    )
    own_total, log_total = group_log_total(local_max, local_sum, points.shape[0])
    other_sums, other_counts = block_sums(other_scores, log_total, members)
    sent_sums = lax.ppermute(other_sums, "dp", swap)
    sent_counts = lax.ppermute(other_counts, "dp", swap)
    own_sums, own_counts = block_sums(own_scores, log_total, members)
    sums = own_sums + sent_sums
    counts = own_counts + sent_counts
    new_centroids = (sums + centroids) / (counts[:, None] + 1.0)
    return (new_centroids, own_total)


def solution(mesh):
    placed = (P(("dp", "cent"), None), P(("dp", "cent"), None))
    return jax.shard_map(
        on_device,
        mesh=mesh,
        in_specs=placed,
        out_specs=(P(("dp", "cent"), None), P(("dp", "cent"))),
        check_vma=False,
    )
```

```python
import math

import jax
import jax.numpy as jnp
from jax import lax
from jax.sharding import PartitionSpec as P

HALVES = 2


def score_block(members, cent_block, score_scale):
    sq_norm = jnp.sum(jnp.square(cent_block.astype(jnp.float32)), axis=1)
    products = lax.dot_general(
        members, cent_block, (((1,), (1,)), ((), ())), preferred_element_type=jnp.float32
    )
    return (2.0 * products - sq_norm[None, :]) * score_scale


def merge_stats(first, second):
    top = jnp.maximum(first[0], second[0])
    total = first[1] * jnp.exp(first[0] - top) + second[1] * jnp.exp(second[0] - top)
    return jnp.stack([top, total])


def group_log_total(local_max, local_sum):
    cent_count = lax.axis_size("cent")
    stats = jnp.stack([local_max, local_sum])
    bit = 1
    while bit < cent_count:
        partner = lax.ppermute(stats, "cent", [(i, i ^ bit) for i in range(cent_count)])
        stats = merge_stats(stats, partner)
        bit *= 2
    return stats[0] + jnp.log(stats[1])


def on_device(points, centroids):
    feature_width = centroids.shape[1]
    own_points = points.shape[0]
    score_scale = 7.0 / math.sqrt(feature_width)
    swap = [(0, 1), (1, 0)]
    copies = centroids.astype(jnp.bfloat16)
    members = lax.all_gather(points, "cent", axis=0, tiled=True)
    other_copies = lax.ppermute(copies, "dp", swap)
    both = jnp.concatenate([other_copies, copies], axis=0)
    own_rows = copies.shape[0]
    span = members.shape[0] // HALVES
    halves = [members[index_h * span : (index_h + 1) * span] for index_h in range(HALVES)]
    scores = [score_block(half, both, score_scale) for half in halves]
    totals = []
    for part in scores:
        local_max = jnp.max(part, axis=1)
        local_sum = jnp.sum(jnp.exp(part - local_max[:, None]), axis=1)
        totals.append(group_log_total(local_max, local_sum))
    sums = None
    counts = None
    for part, total, half in zip(scores, totals, halves):
        weights = jnp.exp(part - total[:, None]).astype(jnp.bfloat16)
        part_sums = lax.dot_general(
            weights, half, (((0,), (0,)), ((), ())), preferred_element_type=jnp.float32
        )
        part_counts = jnp.sum(weights, axis=0, dtype=jnp.float32)
        sums = part_sums if sums is None else sums + part_sums
        counts = part_counts if counts is None else counts + part_counts
    sent_sums = lax.ppermute(sums[:own_rows], "dp", swap)
    sent_counts = lax.ppermute(counts[:own_rows], "dp", swap)
    own_sums = sums[own_rows:] + sent_sums
    own_counts = counts[own_rows:] + sent_counts
    new_centroids = (own_sums + centroids) / (own_counts[:, None] + 1.0)
    log_total = jnp.concatenate(totals)
    own_total = lax.dynamic_slice_in_dim(log_total, lax.axis_index("cent") * own_points, own_points)
    return (new_centroids, own_total)


def solution(mesh):
    placed = (P(("dp", "cent"), None), P(("dp", "cent"), None))
    return jax.shard_map(
        on_device,
        mesh=mesh,
        in_specs=placed,
        out_specs=(P(("dp", "cent"), None), P(("dp", "cent"))),
        check_vma=False,
    )
```

```python
import math

import jax
import jax.numpy as jnp
from jax import lax
from jax.sharding import PartitionSpec as P

HALVES = 2


def score_block(members, cent_block, score_scale):
    sq_norm = jnp.sum(jnp.square(cent_block.astype(jnp.float32)), axis=1)
    products = lax.dot_general(
        members, cent_block, (((1,), (1,)), ((), ())), preferred_element_type=jnp.float32
    )
    return (2.0 * products - sq_norm[None, :]) * score_scale


def merge_stats(first, second):
    top = jnp.maximum(first[0], second[0])
    total = first[1] * jnp.exp(first[0] - top) + second[1] * jnp.exp(second[0] - top)
    return jnp.stack([top, total])


def group_log_total(local_max, local_sum):
    cent_count = lax.axis_size("cent")
    stats = jnp.stack([local_max, local_sum])
    bit = 1
    while bit < cent_count:
        partner = lax.ppermute(stats, "cent", [(i, i ^ bit) for i in range(cent_count)])
        stats = merge_stats(stats, partner)
        bit *= 2
    return stats[0] + jnp.log(stats[1])


def on_device(points, centroids):
    feature_width = centroids.shape[1]
    own_points = points.shape[0]
    score_scale = 7.0 / math.sqrt(feature_width)
    swap = [(0, 1), (1, 0)]
    copies = centroids.astype(jnp.bfloat16)
    members = lax.all_gather(points, "cent", axis=0, tiled=True)
    other_copies = lax.ppermute(copies, "dp", swap)
    both = jnp.concatenate([other_copies, copies], axis=0)
    own_rows = copies.shape[0]
    span = members.shape[0] // HALVES
    halves = [members[index_h * span : (index_h + 1) * span] for index_h in range(HALVES)]
    scores = [score_block(half, both, score_scale) for half in halves]
    local_max = jnp.concatenate([jnp.max(part, axis=1) for part in scores])
    local_sum = jnp.concatenate(
        [jnp.sum(jnp.exp(part - top[:, None]), axis=1) for part, top in zip(scores, jnp.split(local_max, HALVES))]
    )
    log_total = group_log_total(local_max, local_sum)
    totals = jnp.split(log_total, HALVES)
    sums = None
    counts = None
    for part, total, half in zip(scores, totals, halves):
        weights = jnp.exp(part - total[:, None]).astype(jnp.bfloat16)
        part_sums = lax.dot_general(
            weights, half, (((0,), (0,)), ((), ())), preferred_element_type=jnp.float32
        )
        part_counts = jnp.sum(weights, axis=0, dtype=jnp.float32)
        sums = part_sums if sums is None else sums + part_sums
        counts = part_counts if counts is None else counts + part_counts
    sent_sums = lax.ppermute(sums[:own_rows], "dp", swap)
    sent_counts = lax.ppermute(counts[:own_rows], "dp", swap)
    own_sums = sums[own_rows:] + sent_sums
    own_counts = counts[own_rows:] + sent_counts
    new_centroids = (own_sums + centroids) / (own_counts[:, None] + 1.0)
    own_total = lax.dynamic_slice_in_dim(log_total, lax.axis_index("cent") * own_points, own_points)
    return (new_centroids, own_total)


def solution(mesh):
    placed = (P(("dp", "cent"), None), P(("dp", "cent"), None))
    return jax.shard_map(
        on_device,
        mesh=mesh,
        in_specs=placed,
        out_specs=(P(("dp", "cent"), None), P(("dp", "cent"))),
        check_vma=False,
    )
```

```python
import functools
import math

import jax
import jax.numpy as jnp
from jax import lax
from jax.experimental import pallas as pl
from jax.experimental.pallas import tpu as pltpu
from jax.sharding import PartitionSpec as P

HALVES = 2
TILE = 512


def _stats_kernel(x_ref, c_ref, n_ref, m_ref, l_ref, *, scale):
    s = lax.dot_general(
        c_ref[...], x_ref[...], (((1,), (1,)), ((), ())), preferred_element_type=jnp.float32
    )
    s = (2.0 * s - n_ref[...]) * scale
    top = jnp.max(s, axis=0, keepdims=True)
    m_ref[0] = top
    l_ref[0] = jnp.sum(jnp.exp(s - top), axis=0, keepdims=True)


def point_stats(x, c, norm_col, scale):
    rows, width = x.shape
    cents = c.shape[0]
    steps = rows // TILE
    out = jax.ShapeDtypeStruct((steps, 1, TILE), jnp.float32)
    m, l = pl.pallas_call(
        functools.partial(_stats_kernel, scale=scale),
        grid=(steps,),
        in_specs=[
            pl.BlockSpec((TILE, width), lambda i: (i, 0)),
            pl.BlockSpec((cents, width), lambda i: (0, 0)),
            pl.BlockSpec((cents, 1), lambda i: (0, 0)),
        ],
        out_specs=[
            pl.BlockSpec((1, 1, TILE), lambda i: (i, 0, 0)),
            pl.BlockSpec((1, 1, TILE), lambda i: (i, 0, 0)),
        ],
        out_shape=[out, out],
    )(x, c, norm_col)
    return m.reshape(rows), l.reshape(rows)


def _sums_kernel(x_ref, c_ref, n_ref, t_ref, s_ref, k_ref, *, scale):
    @pl.when(pl.program_id(0) == 0)
    def _():
        s_ref[...] = jnp.zeros_like(s_ref)
        k_ref[...] = jnp.zeros_like(k_ref)

    x = x_ref[...]
    s = lax.dot_general(
        c_ref[...], x, (((1,), (1,)), ((), ())), preferred_element_type=jnp.float32
    )
    s = (2.0 * s - n_ref[...]) * scale
    w = jnp.exp(s - t_ref[0]).astype(jnp.bfloat16)
    s_ref[...] += lax.dot_general(
        w, x, (((1,), (0,)), ((), ())), preferred_element_type=jnp.float32
    )
    k_ref[...] += jnp.sum(w.astype(jnp.float32), axis=1, keepdims=True)


def weighted_sums(x, c, norm_col, log_total, scale):
    rows, width = x.shape
    cents = c.shape[0]
    steps = rows // TILE
    sums, counts = pl.pallas_call(
        functools.partial(_sums_kernel, scale=scale),
        grid=(steps,),
        in_specs=[
            pl.BlockSpec((TILE, width), lambda i: (i, 0)),
            pl.BlockSpec((cents, width), lambda i: (0, 0)),
            pl.BlockSpec((cents, 1), lambda i: (0, 0)),
            pl.BlockSpec((1, 1, TILE), lambda i: (i, 0, 0)),
        ],
        out_specs=[
            pl.BlockSpec((cents, width), lambda i: (0, 0)),
            pl.BlockSpec((cents, 1), lambda i: (0, 0)),
        ],
        out_shape=[
            jax.ShapeDtypeStruct((cents, width), jnp.float32),
            jax.ShapeDtypeStruct((cents, 1), jnp.float32),
        ],
        compiler_params=pltpu.CompilerParams(dimension_semantics=("arbitrary",)),
    )(x, c, norm_col, log_total.reshape(steps, 1, TILE))
    return sums, counts.reshape(cents)


def merge_stats(first, second):
    top = jnp.maximum(first[0], second[0])
    total = first[1] * jnp.exp(first[0] - top) + second[1] * jnp.exp(second[0] - top)
    return jnp.stack([top, total])


def group_log_total(local_max, local_sum):
    cent_count = lax.axis_size("cent")
    stats = jnp.stack([local_max, local_sum])
    bit = 1
    while bit < cent_count:
        partner = lax.ppermute(stats, "cent", [(i, i ^ bit) for i in range(cent_count)])
        stats = merge_stats(stats, partner)
        bit *= 2
    return stats[0] + jnp.log(stats[1])


def on_device(points, centroids):
    feature_width = centroids.shape[1]
    own_points = points.shape[0]
    score_scale = 7.0 / math.sqrt(feature_width)
    swap = [(0, 1), (1, 0)]
    copies = centroids.astype(jnp.bfloat16)
    members = lax.all_gather(points, "cent", axis=0, tiled=True)
    other_copies = lax.ppermute(copies, "dp", swap)
    both = jnp.concatenate([other_copies, copies], axis=0)
    norm_col = jnp.sum(jnp.square(both.astype(jnp.float32)), axis=1, keepdims=True)
    own_rows = copies.shape[0]
    span = members.shape[0] // HALVES
    halves = [members[index_h * span : (index_h + 1) * span] for index_h in range(HALVES)]
    totals = []
    for half in halves:
        local_max, local_sum = point_stats(half, both, norm_col, score_scale)
        totals.append(group_log_total(local_max, local_sum))
    sums = None
    counts = None
    for total, half in zip(totals, halves):
        part_sums, part_counts = weighted_sums(half, both, norm_col, total, score_scale)
        sums = part_sums if sums is None else sums + part_sums
        counts = part_counts if counts is None else counts + part_counts
    sent_sums = lax.ppermute(sums[:own_rows], "dp", swap)
    sent_counts = lax.ppermute(counts[:own_rows], "dp", swap)
    own_sums = sums[own_rows:] + sent_sums
    own_counts = counts[own_rows:] + sent_counts
    new_centroids = (own_sums + centroids) / (own_counts[:, None] + 1.0)
    log_total = jnp.concatenate(totals)
    own_total = lax.dynamic_slice_in_dim(log_total, lax.axis_index("cent") * own_points, own_points)
    return (new_centroids, own_total)


def solution(mesh):
    placed = (P(("dp", "cent"), None), P(("dp", "cent"), None))
    return jax.shard_map(
        on_device,
        mesh=mesh,
        in_specs=placed,
        out_specs=(P(("dp", "cent"), None), P(("dp", "cent"))),
        check_vma=False,
    )
```

```python
import math

import jax
import jax.numpy as jnp
from jax import lax
from jax.sharding import PartitionSpec as P

LEAD_PARTS = 4


def score_block(members, cent_block, score_scale):
    sq_norm = jnp.sum(jnp.square(cent_block.astype(jnp.float32)), axis=1)
    products = lax.dot_general(
        members, cent_block, (((1,), (1,)), ((), ())), preferred_element_type=jnp.float32
    )
    return (2.0 * products - sq_norm[None, :]) * score_scale


def merge_stats(first, second):
    top = jnp.maximum(first[0], second[0])
    total = first[1] * jnp.exp(first[0] - top) + second[1] * jnp.exp(second[0] - top)
    return jnp.stack([top, total])


def group_log_total(local_max, local_sum):
    cent_count = lax.axis_size("cent")
    stats = jnp.stack([local_max, local_sum])
    bit = 1
    while bit < cent_count:
        partner = lax.ppermute(stats, "cent", [(i, i ^ bit) for i in range(cent_count)])
        stats = merge_stats(stats, partner)
        bit *= 2
    return stats[0] + jnp.log(stats[1])


def on_device(points, centroids):
    feature_width = centroids.shape[1]
    own_points = points.shape[0]
    score_scale = 7.0 / math.sqrt(feature_width)
    swap = [(0, 1), (1, 0)]
    copies = centroids.astype(jnp.bfloat16)
    members = lax.all_gather(points, "cent", axis=0, tiled=True)
    other_copies = lax.ppermute(copies, "dp", swap)
    both = jnp.concatenate([other_copies, copies], axis=0)
    own_rows = copies.shape[0]
    lead = members.shape[0] // LEAD_PARTS
    halves = [members[:lead], members[lead:]]
    scores = [score_block(half, both, score_scale) for half in halves]
    totals = []
    for part in scores:
        local_max = jnp.max(part, axis=1)
        local_sum = jnp.sum(jnp.exp(part - local_max[:, None]), axis=1)
        totals.append(group_log_total(local_max, local_sum))
    sums = None
    counts = None
    for part, total, half in zip(scores, totals, halves):
        weights = jnp.exp(part - total[:, None]).astype(jnp.bfloat16)
        part_sums = lax.dot_general(
            weights, half, (((0,), (0,)), ((), ())), preferred_element_type=jnp.float32
        )
        part_counts = jnp.sum(weights, axis=0, dtype=jnp.float32)
        sums = part_sums if sums is None else sums + part_sums
        counts = part_counts if counts is None else counts + part_counts
    sent_sums = lax.ppermute(sums[:own_rows], "dp", swap)
    sent_counts = lax.ppermute(counts[:own_rows], "dp", swap)
    own_sums = sums[own_rows:] + sent_sums
    own_counts = counts[own_rows:] + sent_counts
    new_centroids = (own_sums + centroids) / (own_counts[:, None] + 1.0)
    log_total = jnp.concatenate(totals)
    own_total = lax.dynamic_slice_in_dim(log_total, lax.axis_index("cent") * own_points, own_points)
    return (new_centroids, own_total)


def solution(mesh):
    placed = (P(("dp", "cent"), None), P(("dp", "cent"), None))
    return jax.shard_map(
        on_device,
        mesh=mesh,
        in_specs=placed,
        out_specs=(P(("dp", "cent"), None), P(("dp", "cent"))),
        check_vma=False,
    )
```

```python
import math

import jax
import jax.numpy as jnp
from jax import lax
from jax.sharding import PartitionSpec as P


HALVES = 2


def score_block(members, cent_block, score_scale):
    sq_norm = jnp.sum(jnp.square(cent_block.astype(jnp.float32)), axis=1)
    products = lax.dot_general(
        members, cent_block, (((1,), (1,)), ((), ())), preferred_element_type=jnp.float32
    )
    return (2.0 * products - sq_norm[None, :]) * score_scale


def merge_stats(first, second):
    top = jnp.maximum(first[0], second[0])
    total = first[1] * jnp.exp(first[0] - top) + second[1] * jnp.exp(second[0] - top)
    return jnp.stack([top, total])


def group_log_total(local_max, local_sum, reverse):
    cent_count = lax.axis_size("cent")
    stats = jnp.stack([local_max, local_sum])
    bits = [1 << k for k in range(cent_count.bit_length() - 1)]
    if reverse:
        bits = bits[::-1]
    for bit in bits:
        partner = lax.ppermute(stats, "cent", [(i, i ^ bit) for i in range(cent_count)])
        stats = merge_stats(stats, partner)
    return stats[0] + jnp.log(stats[1])


def on_device(points, centroids):
    feature_width = centroids.shape[1]
    own_points = points.shape[0]
    score_scale = 7.0 / math.sqrt(feature_width)
    swap = [(0, 1), (1, 0)]
    copies = centroids.astype(jnp.bfloat16)
    members = lax.all_gather(points, "cent", axis=0, tiled=True)
    other_copies = lax.ppermute(copies, "dp", swap)
    both = jnp.concatenate([other_copies, copies], axis=0)
    own_rows = copies.shape[0]
    span = members.shape[0] // HALVES
    halves = [members[index_h * span : (index_h + 1) * span] for index_h in range(HALVES)]
    scores = [score_block(half, both, score_scale) for half in halves]
    totals = []
    for index_h, part in enumerate(scores):
        local_max = jnp.max(part, axis=1)
        local_sum = jnp.sum(jnp.exp(part - local_max[:, None]), axis=1)
        totals.append(group_log_total(local_max, local_sum, index_h % 2 == 1))
    sums = None
    counts = None
    for part, total, half in zip(scores, totals, halves):
        weights = jnp.exp(part - total[:, None]).astype(jnp.bfloat16)
        part_sums = lax.dot_general(
            weights, half, (((0,), (0,)), ((), ())), preferred_element_type=jnp.float32
        )
        part_counts = jnp.sum(weights, axis=0, dtype=jnp.float32)
        sums = part_sums if sums is None else sums + part_sums
        counts = part_counts if counts is None else counts + part_counts
    sent_sums = lax.ppermute(sums[:own_rows], "dp", swap)
    sent_counts = lax.ppermute(counts[:own_rows], "dp", swap)
    own_sums = sums[own_rows:] + sent_sums
    own_counts = counts[own_rows:] + sent_counts
    new_centroids = (own_sums + centroids) / (own_counts[:, None] + 1.0)
    log_total = jnp.concatenate(totals)
    own_total = lax.dynamic_slice_in_dim(log_total, lax.axis_index("cent") * own_points, own_points)
    return (new_centroids, own_total)


def solution(mesh):
    placed = (P(("dp", "cent"), None), P(("dp", "cent"), None))
    return jax.shard_map(
        on_device,
        mesh=mesh,
        in_specs=placed,
        out_specs=(P(("dp", "cent"), None), P(("dp", "cent"))),
        check_vma=False,
    )
```

```python
import math

import jax
import jax.numpy as jnp
from jax import lax
from jax.sharding import PartitionSpec as P


HALVES = 2
COUNT_LANES = 128


def score_block(members, cent_block, score_scale):
    sq_norm = jnp.sum(jnp.square(cent_block.astype(jnp.float32)), axis=1)
    products = lax.dot_general(
        members, cent_block, (((1,), (1,)), ((), ())), preferred_element_type=jnp.float32
    )
    return (2.0 * products - sq_norm[None, :]) * score_scale


def merge_stats(first, second):
    top = jnp.maximum(first[0], second[0])
    total = first[1] * jnp.exp(first[0] - top) + second[1] * jnp.exp(second[0] - top)
    return jnp.stack([top, total])


def group_log_total(local_max, local_sum):
    cent_count = lax.axis_size("cent")
    stats = jnp.stack([local_max, local_sum])
    bit = 1
    while bit < cent_count:
        partner = lax.ppermute(stats, "cent", [(i, i ^ bit) for i in range(cent_count)])
        stats = merge_stats(stats, partner)
        bit *= 2
    return stats[0] + jnp.log(stats[1])


def on_device(points, centroids):
    feature_width = centroids.shape[1]
    own_points = points.shape[0]
    score_scale = 7.0 / math.sqrt(feature_width)
    swap = [(0, 1), (1, 0)]
    copies = centroids.astype(jnp.bfloat16)
    members = lax.all_gather(points, "cent", axis=0, tiled=True)
    other_copies = lax.ppermute(copies, "dp", swap)
    both = jnp.concatenate([other_copies, copies], axis=0)
    own_rows = copies.shape[0]
    span = members.shape[0] // HALVES
    halves = [members[index_h * span : (index_h + 1) * span] for index_h in range(HALVES)]
    scores = [score_block(half, both, score_scale) for half in halves]
    totals = []
    for part in scores:
        local_max = jnp.max(part, axis=1)
        local_sum = jnp.sum(jnp.exp(part - local_max[:, None]), axis=1)
        totals.append(group_log_total(local_max, local_sum))
    sums = None
    counts = None
    for part, total, half in zip(scores, totals, halves):
        weights = jnp.exp(part - total[:, None]).astype(jnp.bfloat16)
        extended = jnp.concatenate(
            [half, jnp.ones((half.shape[0], COUNT_LANES), half.dtype)], axis=1
        )
        both_sums = lax.dot_general(
            weights, extended, (((0,), (0,)), ((), ())), preferred_element_type=jnp.float32
        )
        part_sums = both_sums[:, : half.shape[1]]
        part_counts = both_sums[:, half.shape[1]]
        sums = part_sums if sums is None else sums + part_sums
        counts = part_counts if counts is None else counts + part_counts
    sent_sums = lax.ppermute(sums[:own_rows], "dp", swap)
    sent_counts = lax.ppermute(counts[:own_rows], "dp", swap)
    own_sums = sums[own_rows:] + sent_sums
    own_counts = counts[own_rows:] + sent_counts
    new_centroids = (own_sums + centroids) / (own_counts[:, None] + 1.0)
    log_total = jnp.concatenate(totals)
    own_total = lax.dynamic_slice_in_dim(log_total, lax.axis_index("cent") * own_points, own_points)
    return (new_centroids, own_total)


def solution(mesh):
    placed = (P(("dp", "cent"), None), P(("dp", "cent"), None))
    return jax.shard_map(
        on_device,
        mesh=mesh,
        in_specs=placed,
        out_specs=(P(("dp", "cent"), None), P(("dp", "cent"))),
        check_vma=False,
    )
```

```python
import math

import jax
import jax.numpy as jnp
from jax import lax
from jax.sharding import PartitionSpec as P


HALVES = 2


def score_block(members, cent_block, score_scale):
    sq_norm = jnp.sum(jnp.square(cent_block.astype(jnp.float32)), axis=1)
    products = lax.dot_general(
        members, cent_block, (((1,), (1,)), ((), ())), preferred_element_type=jnp.float32
    )
    return (2.0 * products - sq_norm[None, :]) * score_scale


def merge_stats(parts):
    tops = jnp.stack([part[0] for part in parts])
    sums = jnp.stack([part[1] for part in parts])
    top = jnp.max(tops, axis=0)
    total = jnp.sum(sums * jnp.exp(tops - top[None]), axis=0)
    return jnp.stack([top, total])


def group_log_total(local_max, local_sum):
    cent_count = lax.axis_size("cent")
    stats = jnp.stack([local_max, local_sum])
    bit = 1
    while bit < cent_count:
        masks = [bit, 2 * bit, 3 * bit] if 2 * bit < cent_count else [bit]
        parts = [stats] + [
            lax.ppermute(stats, "cent", [(i, i ^ mask) for i in range(cent_count)])
            for mask in masks
        ]
        stats = merge_stats(parts)
        bit *= 4 if len(masks) == 3 else 2
    return stats[0] + jnp.log(stats[1])


def on_device(points, centroids):
    feature_width = centroids.shape[1]
    own_points = points.shape[0]
    score_scale = 7.0 / math.sqrt(feature_width)
    swap = [(0, 1), (1, 0)]
    copies = centroids.astype(jnp.bfloat16)
    members = lax.all_gather(points, "cent", axis=0, tiled=True)
    other_copies = lax.ppermute(copies, "dp", swap)
    both = jnp.concatenate([other_copies, copies], axis=0)
    own_rows = copies.shape[0]
    span = members.shape[0] // HALVES
    halves = [members[index_h * span : (index_h + 1) * span] for index_h in range(HALVES)]
    scores = [score_block(half, both, score_scale) for half in halves]
    totals = []
    for part in scores:
        local_max = jnp.max(part, axis=1)
        local_sum = jnp.sum(jnp.exp(part - local_max[:, None]), axis=1)
        totals.append(group_log_total(local_max, local_sum))
    sums = None
    counts = None
    for part, total, half in zip(scores, totals, halves):
        weights = jnp.exp(part - total[:, None]).astype(jnp.bfloat16)
        part_sums = lax.dot_general(
            weights, half, (((0,), (0,)), ((), ())), preferred_element_type=jnp.float32
        )
        part_counts = jnp.sum(weights, axis=0, dtype=jnp.float32)
        sums = part_sums if sums is None else sums + part_sums
        counts = part_counts if counts is None else counts + part_counts
    sent_sums = lax.ppermute(sums[:own_rows], "dp", swap)
    sent_counts = lax.ppermute(counts[:own_rows], "dp", swap)
    own_sums = sums[own_rows:] + sent_sums
    own_counts = counts[own_rows:] + sent_counts
    new_centroids = (own_sums + centroids) / (own_counts[:, None] + 1.0)
    log_total = jnp.concatenate(totals)
    own_total = lax.dynamic_slice_in_dim(log_total, lax.axis_index("cent") * own_points, own_points)
    return (new_centroids, own_total)


def solution(mesh):
    placed = (P(("dp", "cent"), None), P(("dp", "cent"), None))
    return jax.shard_map(
        on_device,
        mesh=mesh,
        in_specs=placed,
        out_specs=(P(("dp", "cent"), None), P(("dp", "cent"))),
        check_vma=False,
    )
```

```python
import math

import jax
import jax.numpy as jnp
from jax import lax
from jax.sharding import PartitionSpec as P


HALVES = 2


def score_block(members, cent_block, score_scale):
    sq_norm = jnp.sum(jnp.square(cent_block.astype(jnp.float32)), axis=1)
    products = lax.dot_general(
        members, cent_block, (((1,), (1,)), ((), ())), preferred_element_type=jnp.float32
    )
    return (2.0 * products - sq_norm[None, :]) * score_scale


def merge_stats(first, second):
    top = jnp.maximum(first[0], second[0])
    total = first[1] * jnp.exp(first[0] - top) + second[1] * jnp.exp(second[0] - top)
    return jnp.stack([top, total])


def group_log_total(local_max, local_sum):
    cent_count = lax.axis_size("cent")
    stats = jnp.stack([local_max, local_sum])
    bit = 1
    while bit < cent_count:
        masks = [bit, 3 * bit] if 2 * bit < cent_count else [bit]
        for mask in masks:
            partner = lax.ppermute(stats, "cent", [(i, i ^ mask) for i in range(cent_count)])
            stats = merge_stats(stats, partner)
        bit *= 2 * len(masks)
    return stats[0] + jnp.log(stats[1])


def on_device(points, centroids):
    feature_width = centroids.shape[1]
    own_points = points.shape[0]
    score_scale = 7.0 / math.sqrt(feature_width)
    swap = [(0, 1), (1, 0)]
    copies = centroids.astype(jnp.bfloat16)
    members = lax.all_gather(points, "cent", axis=0, tiled=True)
    other_copies = lax.ppermute(copies, "dp", swap)
    both = jnp.concatenate([other_copies, copies], axis=0)
    own_rows = copies.shape[0]
    span = members.shape[0] // HALVES
    halves = [members[index_h * span : (index_h + 1) * span] for index_h in range(HALVES)]
    scores = [score_block(half, both, score_scale) for half in halves]
    totals = []
    for part in scores:
        local_max = jnp.max(part, axis=1)
        local_sum = jnp.sum(jnp.exp(part - local_max[:, None]), axis=1)
        totals.append(group_log_total(local_max, local_sum))
    sums = None
    counts = None
    for part, total, half in zip(scores, totals, halves):
        weights = jnp.exp(part - total[:, None]).astype(jnp.bfloat16)
        part_sums = lax.dot_general(
            weights, half, (((0,), (0,)), ((), ())), preferred_element_type=jnp.float32
        )
        part_counts = jnp.sum(weights, axis=0, dtype=jnp.float32)
        sums = part_sums if sums is None else sums + part_sums
        counts = part_counts if counts is None else counts + part_counts
    sent_sums = lax.ppermute(sums[:own_rows], "dp", swap)
    sent_counts = lax.ppermute(counts[:own_rows], "dp", swap)
    own_sums = sums[own_rows:] + sent_sums
    own_counts = counts[own_rows:] + sent_counts
    new_centroids = (own_sums + centroids) / (own_counts[:, None] + 1.0)
    log_total = jnp.concatenate(totals)
    own_total = lax.dynamic_slice_in_dim(log_total, lax.axis_index("cent") * own_points, own_points)
    return (new_centroids, own_total)


def solution(mesh):
    placed = (P(("dp", "cent"), None), P(("dp", "cent"), None))
    return jax.shard_map(
        on_device,
        mesh=mesh,
        in_specs=placed,
        out_specs=(P(("dp", "cent"), None), P(("dp", "cent"))),
        check_vma=False,
    )
```
